256 devices in a mesh: seq: 64 (over y, z, core), ch: 4 (over x).
Axes of the slice: x: 4, y: 4, z: 8, core: 2. Of those that a mesh axis runs over, the one named last changes fastest.
Arguments:
- query_stream: bfloat16 [16384, 4096], P('seq', 'ch'), may hold values from -16 to 16
- key_stream: bfloat16 [16384, 4096], P('seq', 'ch'), may hold values from -6 to 6
- value_stream: bfloat16 [16384, 4096], P('seq', 'ch'), may hold values from -6 to 6
- filter_taps: float32 [4096, 128], P('ch'), may hold values from -0.5 to 0.5
- out_weight: bfloat16 [4096, 4096], P('seq', 'ch'), may hold values from -0.09375 to 0.09375
- upstream: bfloat16 [16384, 4096], P('seq', 'ch'), may hold values from -6 to 6
Outputs:
- mixed: bfloat16 [16384, 4096], P('seq', 'ch')
- grad_query: bfloat16 [16384, 4096], P('seq', 'ch')
- grad_key: bfloat16 [16384, 4096], P('seq', 'ch')
- grad_value: bfloat16 [16384, 4096], P('seq', 'ch')
- grad_filter: float32 [4096, 128], P('ch')
- grad_weight: float32 [4096, 4096], P('seq', 'ch')
The draws below stay inside these ranges and needn't reach their ends.
All inputs are finite; a program needn't handle non-finite values.
Results may differ from the reference program's by a relative error of at most 0.0057.
Values may be sent and summed in bfloat16 or wider, within the bound.
No kernel may reach another device: no remote copies, remote signals or barrier semaphores. Data moves between devices by JAX's collectives and lax.ppermute only.
A program may use at most 128 MiB of HBM per device.

```python
import jax
import jax.numpy as jnp
from jax import lax

WIDTH = 4096
CHANNELS = 4096
TAPS = 128
LENGTH = 16384


def with_spikes(result, own_key, source, target, parts, factor):
    def block_of(position):
        return (jnp.arange(result.shape[position]) // (result.shape[position] // parts)).reshape((-1,) + (1,) * (result.ndim - 1 - position))

    one_side = jax.random.permutation(own_key, parts)[block_of(target)]
    other_side = (block_of(target) + parts // 2) % parts
    return jnp.where((block_of(source) == one_side) | (block_of(source) == other_side), factor * result, result)


def level_of(own_key, extent, split, low, high):
    gain = 1.0
    for dim, parts in split:
        draws = jax.random.uniform(jax.random.fold_in(jax.random.fold_in(own_key, 6), dim), (parts,), jnp.float32, low / len(split), high / len(split))
        gain = gain * jnp.repeat(jnp.exp(draws), extent[dim] // parts).reshape((-1,) + (1,) * (len(extent) - 1 - dim))
    return gain


def bell_draw(stream_key, extent, spread, reach, split=(), kind=jnp.bfloat16):
    drawn = jax.random.normal(stream_key, extent, jnp.float32) * spread
    if len(split) > 0:
        drawn = level_of(stream_key, extent, split, -0.22, 0.18) * drawn
    return jnp.clip(drawn, min=-reach, max=reach).astype(kind)


def gaussian_with(stream_key, extent, spread, limit, cuts, heavy, kind=jnp.bfloat16):
    values = spread * jax.random.normal(stream_key, extent, jnp.float32)
    if cuts:
        values = values * level_of(stream_key, extent, cuts, -0.22, 0.18)
    return jnp.clip(with_spikes(values, jax.random.fold_in(stream_key, 3), *heavy), -limit, limit).astype(kind)


def setup_inputs(seed: int = 0) -> dict:
    keys = jax.random.split(jax.random.key(seed), 7)
    return {
        "query_stream": gaussian_with(keys[0], (LENGTH, CHANNELS), 1.0, 16.0, ((0, 64), (1, 4)), (0, 1, 64, 4.0)),
        "key_stream": bell_draw(keys[1], (LENGTH, CHANNELS), 1.0, 6.0, ((0, 64), (1, 4))),
        "value_stream": bell_draw(keys[2], (LENGTH, CHANNELS), 1.0, 6.0, ((0, 64), (1, 4))),
        "filter_taps": bell_draw(keys[3], (CHANNELS, TAPS), TAPS ** -0.5, 0.5, ((0, 4),), jnp.float32),
        "out_weight": bell_draw(keys[4], (CHANNELS, WIDTH), CHANNELS ** -0.5, 0.09375, ((0, 64), (1, 4))),
        "upstream": bell_draw(keys[5], (LENGTH, WIDTH), 1.0, 6.0, ((0, 64), (1, 4))),
    }


def reference(query_stream, key_stream, value_stream, filter_taps, out_weight, upstream):
    length = query_stream.shape[0]
    keyed = (key_stream.astype(jnp.float32) * value_stream.astype(jnp.float32)).astype(jnp.bfloat16)
    front_pad = jnp.concatenate([jnp.zeros((TAPS - 1, CHANNELS), jnp.float32), keyed.astype(jnp.float32)], axis=0)

    def forward_tap(index, accum):
        shifted = lax.dynamic_slice_in_dim(front_pad, TAPS - 1 - index, length, 0)
        column = lax.dynamic_slice_in_dim(filter_taps, index, 1, 1)[:, 0]
        return accum + column[None, :] * shifted

    response = lax.fori_loop(jnp.int32(0), jnp.int32(TAPS), forward_tap, jnp.zeros((length, CHANNELS), jnp.float32))
    gated = (query_stream.astype(jnp.float32) * response).astype(jnp.bfloat16)
    mixed = jnp.dot(gated, out_weight, preferred_element_type=jnp.float32).astype(jnp.bfloat16)
    grad_gated = jnp.dot(upstream, out_weight.T, preferred_element_type=jnp.float32)
    grad_query = (grad_gated * response).astype(jnp.bfloat16)
    grad_response = grad_gated * query_stream.astype(jnp.float32)
    back_pad = jnp.concatenate([grad_response, jnp.zeros((TAPS - 1, CHANNELS), jnp.float32)], axis=0)

    def backward_tap(index, accum):
        shifted = lax.dynamic_slice_in_dim(back_pad, index, length, 0)
        column = lax.dynamic_slice_in_dim(filter_taps, index, 1, 1)[:, 0]
        return accum + column[None, :] * shifted

    grad_keyed = lax.fori_loop(jnp.int32(0), jnp.int32(TAPS), backward_tap, jnp.zeros((length, CHANNELS), jnp.float32))
    grad_key = (grad_keyed * value_stream.astype(jnp.float32)).astype(jnp.bfloat16)
    grad_value = (grad_keyed * key_stream.astype(jnp.float32)).astype(jnp.bfloat16)

    def tap_gradient(index):
        shifted = lax.dynamic_slice_in_dim(front_pad, TAPS - 1 - index, length, 0)
        return jnp.sum(grad_response * shifted, axis=0)

    grad_filter = lax.map(tap_gradient, jnp.arange(TAPS, dtype=jnp.int32)).T
    grad_weight = lax.dot_general(gated, upstream, (((0,), (0,)), ((), ())), preferred_element_type=jnp.float32)
    return mixed, grad_query, grad_key, grad_value, grad_filter, grad_weight
```

```python
import jax
import jax.numpy as jnp
from jax import lax
from jax.sharding import Mesh
from jax.sharding import PartitionSpec as P

SUB = ("sy", "sz", "sc")


def seq_factors(mesh):
    count = mesh.shape["seq"]
    try:
        devices = list(mesh.devices[:, 0])
        cores = len({d.core_on_chip for d in devices})
        zs = len({d.coords[2] for d in devices})
        if cores * zs and count % (cores * zs) == 0:
            return (count // (cores * zs), zs, cores)
    except Exception:
        pass
    return (count // 16, 8, 2) if count % 16 == 0 else (1, 1, count)


def from_behind(value, axis, count, steps):
    initial, last = (max(0, -steps), min(count, count - steps))
    return lax.ppermute(value, axis, [(source, source + steps) for source in range(initial, last)])


def depthwise(signal, kernel):
    output = lax.conv_general_dilated(
        signal[None],
        kernel[:, None, :],
        (1,),
        "VALID",
        dimension_numbers=("NWC", "WIO", "NWC"),
        feature_group_count=signal.shape[1],
        precision=lax.Precision.HIGHEST,
    )
    return output[0]


def gather_ch(part, count):
    here = lax.axis_index("ch")
    pieces = [part] + [
        lax.ppermute(part, "ch", [(i, (i + k) % count) for i in range(count)]) for k in range(1, count)
    ]
    stacked = jnp.stack(pieces)[(here - jnp.arange(count)) % count]
    return jnp.concatenate([stacked[j] for j in range(count)], axis=1)


def scatter_ch(whole, count):
    here = lax.axis_index("ch")
    width = whole.shape[1] // count
    total = lax.dynamic_slice_in_dim(whole, here * width, width, 1)
    for k in range(1, count):
        block = lax.dynamic_slice_in_dim(whole, ((here + k) % count) * width, width, 1)
        total = total + lax.ppermute(block, "ch", [(i, (i + k) % count) for i in range(count)])
    return total


def butterfly_sum(value, factors):
    for axis, size in zip(SUB, factors):
        bit = 1
        while bit < size:
            value = value + lax.ppermute(value, axis, [(i, i ^ bit) for i in range(size)])
            bit *= 2
    return value


def make_body(factors, chs):
    n_seq = factors[0] * factors[1] * factors[2]

    def body(query_stream, key_stream, value_stream, filter_taps, out_weight, upstream):
        rows_here = query_stream.shape[0]
        tap_count = filter_taps.shape[1]
        keyed = (key_stream.astype(jnp.float32) * value_stream.astype(jnp.float32)).astype(jnp.bfloat16)
        rim_before = from_behind(keyed[rows_here - (tap_count - 1) :], SUB, n_seq, 1)
        front_pad = jnp.concatenate([rim_before, keyed], axis=0).astype(jnp.float32)
        response = depthwise(front_pad, filter_taps.T[::-1])
        query_wide = query_stream.astype(jnp.float32)
        gated = (query_wide * response).astype(jnp.bfloat16)
        gated_full = gather_ch(gated, chs)
        weight_cols = lax.all_gather(out_weight, SUB, axis=0, tiled=True)
        mixed = jnp.dot(gated_full, weight_cols, preferred_element_type=jnp.float32).astype(
            jnp.bfloat16
        )
        partial_terms = lax.dot_general(
            upstream, weight_cols, (((1,), (1,)), ((), ())), preferred_element_type=jnp.float32
        )
        grad_gated = scatter_ch(partial_terms, chs)
        grad_query = (grad_gated * response).astype(jnp.bfloat16)
        grad_response = grad_gated * query_wide
        rim_after = from_behind(grad_response[: tap_count - 1], SUB, n_seq, -1)
        back_pad = jnp.concatenate([grad_response, rim_after], axis=0)
        grad_keyed = depthwise(back_pad, filter_taps.T)
        grad_key = (grad_keyed * value_stream.astype(jnp.float32)).astype(jnp.bfloat16)
        grad_value = (grad_keyed * key_stream.astype(jnp.float32)).astype(jnp.bfloat16)
        filter_local = depthwise(front_pad, grad_response)[::-1].T
        grad_filter = butterfly_sum(filter_local, factors)
        block = out_weight.shape[0]
        columns = lax.slice_in_dim(gated_full, 0, n_seq * block, axis=1)
        columns = columns.reshape((rows_here,) + factors + (block,)).transpose(0, 3, 2, 1, 4)
        columns = columns.reshape(rows_here, n_seq * block)
        partial = lax.dot_general(
            columns, upstream, (((0,), (0,)), ((), ())), preferred_element_type=jnp.float32
        )
        for axis in ("sc", "sz", "sy"):
            partial = lax.psum_scatter(partial, axis, scatter_dimension=0, tiled=True)
        return (mixed, grad_query, grad_key, grad_value, grad_filter, partial)

    return body


def solution(mesh):
    factors = seq_factors(mesh)
    chs = mesh.shape["ch"]
    fine = Mesh(mesh.devices.reshape(factors + (chs,)), SUB + ("ch",))
    rows = P(SUB, "ch")
    in_specs = (rows, rows, rows, P("ch", None), rows, rows)
    out_specs = (rows, rows, rows, rows, P("ch", None), rows)
    return jax.shard_map(
        make_body(factors, chs), mesh=fine, in_specs=in_specs, out_specs=out_specs, check_vma=False
    )
```
